256 devices in a mesh: ctx: 32 (over x, z), head: 8 (over y, core).
Axes of the slice: x: 4, y: 4, z: 8, core: 2. Of those that a mesh axis runs over, the one named last changes fastest.
Arguments:
- features: bfloat16 [8192, 16384], P('ctx', 'head'), may hold values from -6 to 6
- log_decay: float32 [256, 8192], P('head', 'ctx'), may hold values from -2 to 0, as said below
- step_size: float32 [256, 8192], P('head', 'ctx'), may hold values from 0.0002 to 0.002
- b_matrix: bfloat16 [8192, 2048], P('ctx', 'head'), may hold values from -6 to 6
- c_matrix: bfloat16 [8192, 2048], P('ctx', 'head'), may hold values from -6 to 6
- skip_gain: float32 [256], P('head'), may hold values from 0.5 to 1.5
Outputs:
- mixed: bfloat16 [8192, 16384], P('ctx', 'head')
The draws below stay inside these ranges and needn't reach their ends.
Inputs may be any that keep to these rules, and one draw needn't show every extreme that they name: `log_decay`: every entry is negative.
All inputs are finite; a program needn't handle non-finite values.
Results may differ from the reference program's by a relative error of at most 0.0013.
Values sent between devices are 32-bit elements; how exact they have to be, the bound alone decides.
No kernel may reach another device: no remote copies, remote signals or barrier semaphores. Data moves between devices by JAX's collectives and lax.ppermute only.
A program may use at most 320 MiB of HBM per device.

```python
import math
import jax
import jax.numpy as jnp
from jax import lax

H = 256
P_SIZE = 64
N = 256
G = 8
SPAN = 128
BLK = 128
SEQ = 8192
N_CTX = 32


def draw_log_decay(key, part):
    keys = jax.random.split(key, 7)
    share = 0.5
    picker = jax.random.uniform(keys[0], (H,))
    fast_rate = jnp.exp(jax.random.uniform(keys[1], (H,), jnp.float32, math.log(1.0 / 50.0), math.log(1.0 / 30.0)))
    slow_rate = jnp.exp(jax.random.uniform(keys[2], (H,), jnp.float32, math.log(0.02), math.log(0.3))) / SEQ
    decay_speed = jnp.where(picker < share, fast_rate, slow_rate)
    coarse_estimate = jnp.exp(jax.random.uniform(keys[3], (H, SEQ), jnp.float32, math.log(0.5), math.log(1.5)))
    block_multiplier = jnp.exp(jax.random.uniform(keys[4], (H, SEQ // BLK), jnp.float32, math.log(0.5), math.log(2.0)))
    block_multiplier = jnp.repeat(block_multiplier, BLK, axis=1)
    location_list = jax.random.randint(keys[5], (2,), 0, SEQ)
    stack_height = jax.random.uniform(keys[6], (2,), jnp.float32, 0.22, 0.6)
    token_location = jnp.arange(SEQ)
    spike_level = jnp.sum(jnp.where(token_location[None, :] == location_list[:, None], stack_height[:, None], 0.0), axis=0)
    return -(decay_speed[:, None] * coarse_estimate * block_multiplier + spike_level[None, :])


def levels(key, dims, cuts, low, high):
    gain, own = 1.0, jax.random.fold_in(key, 6)
    for position, shards_of in cuts:
        steps = jnp.exp(jax.random.uniform(jax.random.fold_in(own, position), (shards_of,), jnp.float32, low / len(cuts), high / len(cuts)))
        gain = gain * jnp.repeat(steps, dims[position] // shards_of).reshape([-1 if axis == position else 1 for axis in range(len(dims))])
    return gain


def centred(stream_key, extent, deviation, most, cuts=(), kind=jnp.bfloat16):
    entries = deviation * jax.random.normal(stream_key, extent, jnp.float32)
    if cuts:
        entries = entries * levels(stream_key, extent, cuts, -0.22, 0.18)
    return jnp.clip(entries, -most, most).astype(kind)


def setup_inputs(seed: int = 0) -> dict:
    key_list = jax.random.split(jax.random.key(seed), 7)
    features = centred(key_list[0], (SEQ, H * P_SIZE), 1.0, 6.0, ((0, 32), (1, 8)))
    log_decay = draw_log_decay(jax.random.fold_in(key_list[6], 71), 0)
    step_size = jnp.clip(jnp.exp(math.log(0.002) - 2.3025852 * jax.random.uniform(key_list[2], (H, SEQ), jnp.float32) ** levels(key_list[2], (H, SEQ), ((0, 8), (1, 32)), -0.2, 0.2)), 0.0002, 0.002)
    b_matrix = centred(key_list[3], (SEQ, G * N), 1.0, 6.0, ((0, 32), (1, 8)))
    c_matrix = centred(key_list[4], (SEQ, G * N), 1.0, 6.0, ((0, 32), (1, 8)))
    skip_gain = jnp.clip(0.5 + 1.0 * jax.random.uniform(key_list[5], (H,), jnp.float32) ** levels(key_list[5], (H,), ((0, 8),), -0.2, 0.2), 0.5, 1.5)
    return dict(features=features, log_decay=log_decay, step_size=step_size, b_matrix=b_matrix, c_matrix=c_matrix, skip_gain=skip_gain)


def to_sequence(stored):
    blocks = stored.reshape((N_CTX, 2, BLK) + stored.shape[1:])
    return jnp.concatenate([blocks[:, 0], blocks[::-1, 1]], axis=0).reshape(stored.shape)


def to_stored(ordered):
    blocks = ordered.reshape((2 * N_CTX, BLK) + ordered.shape[1:])
    return jnp.stack([blocks[:N_CTX], blocks[N_CTX:][::-1]], axis=1).reshape(ordered.shape)


def reference(features, log_decay, step_size, b_matrix, c_matrix, skip_gain):
    span_count = SEQ // SPAN
    per_group = H // G
    feat_seq = to_sequence(features).reshape(span_count, SPAN, H, P_SIZE)
    decay_seq = to_sequence(log_decay.T).reshape(span_count, SPAN, H)
    step_seq = to_sequence(step_size.T).reshape(span_count, SPAN, H)
    b_seq = to_sequence(b_matrix).reshape(span_count, SPAN, G, N)
    c_seq = to_sequence(c_matrix).reshape(span_count, SPAN, G, N)
    causal = jnp.arange(SPAN)[:, None] >= jnp.arange(SPAN)[None, :]

    def one_span(state, packed):
        inputs, decay, step_rows, b_rows, c_rows = packed
        cumulative = jnp.cumsum(decay, axis=0)
        b_float = b_rows.astype(jnp.float32)
        c_float = c_rows.astype(jnp.float32)
        scores = jnp.einsum("tgn,sgn->tsg", c_float, b_float)
        scores = jnp.repeat(scores, per_group, axis=2)
        decay_gaps = jnp.where(causal[:, :, None], cumulative[:, None, :] - cumulative[None, :, :], -jnp.inf)
        weights = (scores * jnp.exp(decay_gaps) * step_rows[None, :, :]).astype(jnp.bfloat16)
        weights = lax.optimization_barrier(weights)
        diagonal_part = jnp.einsum("tsh,shp->thp", weights.astype(jnp.float32), inputs.astype(jnp.float32))
        state_bf = lax.optimization_barrier(state.astype(jnp.bfloat16))
        state_grouped = state_bf.astype(jnp.float32).reshape(G, per_group, P_SIZE, N)
        state_part = jnp.einsum("tgn,gqpn->tgqp", c_float, state_grouped).reshape(SPAN, H, P_SIZE)
        state_part = state_part * jnp.exp(cumulative)[:, :, None]
        coeffs = jnp.exp(cumulative[-1:] - cumulative) * step_rows
        weighted = (inputs.astype(jnp.float32) * coeffs[:, :, None]).astype(jnp.bfloat16)
        weighted = lax.optimization_barrier(weighted)
        weighted_grouped = weighted.astype(jnp.float32).reshape(SPAN, G, per_group, P_SIZE)
        span_state = jnp.einsum("sgn,sgqp->gqpn", b_float, weighted_grouped).reshape(H, P_SIZE, N)
        new_state = jnp.exp(cumulative[-1])[:, None, None] * state + span_state
        output = diagonal_part + state_part + skip_gain[None, :, None] * inputs.astype(jnp.float32)
        return new_state, output.astype(jnp.bfloat16)

    start = jnp.zeros((H, P_SIZE, N), jnp.float32)
    final_state, outputs = lax.scan(one_span, start, (feat_seq, decay_seq, step_seq, b_seq, c_seq))
    return to_stored(outputs.reshape(SEQ, H * P_SIZE))
```

```python
import jax
import jax.numpy as jnp
from jax import lax
from jax.sharding import PartitionSpec as P

N = 256
SPAN = 128


def carry_by_transpose(block_decay, block_states, axis):
    devices = lax.axis_size(axis)
    _, head_count, head_width, state_size = block_states.shape
    per_chunk = head_count // devices
    flat = head_width * state_size
    pad = 128
    payload = jnp.concatenate(
        [
            block_states.reshape(2, head_count, flat),
            jnp.broadcast_to(block_decay[:, :, None], (2, head_count, pad)),
        ],
        axis=2,
    )
    got = lax.all_to_all(payload, axis, 1, 1, tiled=True)
    got = got.reshape(2, devices, per_chunk, flat + pad)
    chain = jnp.concatenate([got[0], got[1][::-1]], axis=0)
    links = 2 * devices
    decays = chain[:, :, flat]
    states = chain[:, :, :flat]
    q = jnp.arange(links)
    between = (q[None, None, :] > q[None, :, None]) & (q[None, None, :] < q[:, None, None])
    gap = jnp.sum(jnp.where(between[None], jnp.transpose(decays)[:, None, None, :], 0.0), axis=-1)
    lower = q[:, None] > q[None, :]
    mixing = jnp.where(lower[None], jnp.exp(gap), 0.0)
    own = (q[:, None] >= devices) & (q[None, :] == links - 1 - q[:, None])
    solved = jnp.einsum(
        "cqr,rcf->qcf", jnp.where(own[None], 0.0, mixing), states,
        precision=lax.Precision.HIGHEST, preferred_element_type=jnp.float32,
    )
    own_gain = jnp.sum(jnp.where(own[None], mixing, 0.0), axis=2)
    tagged = jnp.concatenate(
        [solved, jnp.broadcast_to(jnp.transpose(own_gain)[:, :, None], (links, per_chunk, pad))],
        axis=2,
    )
    back_out = jnp.stack([tagged[:devices], tagged[devices:][::-1]])
    back_out = back_out.reshape(2, devices * per_chunk, flat + pad)
    got = lax.all_to_all(back_out, axis, 1, 1, tiled=True)
    own_front = block_states[0].reshape(head_count, flat)
    entering = jnp.stack(
        [got[0, :, :flat], got[1, :, :flat] + got[1, :, flat:flat + 1] * own_front]
    )
    return entering.reshape(2, head_count, head_width, state_size)


def on_device(features, log_decay, step_size, b_matrix, c_matrix, skip_gain):
    head_count = log_decay.shape[0]
    tok_rows = features.shape[0]
    head_width = features.shape[1] // head_count
    state_size = N
    group_count = b_matrix.shape[1] // state_size
    per_group = head_count // group_count
    span_count = tok_rows // SPAN
    half_count = span_count // 2
    cumulative = jnp.cumsum(log_decay.reshape(head_count, span_count, SPAN), axis=2)
    step_rows = step_size.reshape(head_count, span_count, SPAN)
    inputs = features.reshape(span_count, SPAN, head_count, head_width)
    grouped_inputs = features.reshape(span_count, SPAN, group_count, per_group, head_width)
    b_spans = b_matrix.reshape(span_count, SPAN, group_count, state_size)
    c_spans = c_matrix.reshape(span_count, SPAN, group_count, state_size)
    scores = jnp.einsum("ktgn,ksgn->gkts", c_spans, b_spans, preferred_element_type=jnp.float32)
    causal = jnp.arange(SPAN)[:, None] >= jnp.arange(SPAN)[None, :]
    cum_grouped = cumulative.reshape(group_count, per_group, span_count, SPAN)
    step_grouped = step_rows.reshape(group_count, per_group, span_count, SPAN)
    decay_gaps = jnp.where(causal, cum_grouped[..., :, None] - cum_grouped[..., None, :], -jnp.inf)
    weights = (scores[:, None] * jnp.exp(decay_gaps) * step_grouped[:, :, :, None, :]).astype(
        jnp.bfloat16
    )
    diagonal_part = jnp.einsum(
        "gqkts,ksgqp->ktgqp", weights, grouped_inputs, preferred_element_type=jnp.float32
    )
    diagonal_part = diagonal_part.reshape(span_count, SPAN, head_count, head_width)
    span_ends = cumulative[:, :, -1]
    coeffs = jnp.exp(span_ends[:, :, None] - cumulative) * step_rows
    weighted = (inputs * jnp.transpose(coeffs, (1, 2, 0))[:, :, :, None]).astype(jnp.bfloat16)
    weighted = weighted.reshape(span_count, SPAN, group_count, per_group, head_width)
    span_states = jnp.einsum(
        "ksgn,ksgqp->kgqpn", b_spans, weighted, preferred_element_type=jnp.float32
    )
    span_states = span_states.reshape(span_count, head_count, head_width, state_size)
    totals = jnp.transpose(span_ends).reshape(2, half_count, head_count)
    grouped = span_states.reshape(2, half_count, head_count, head_width, state_size)

    def advance(running, element):
        return (jnp.exp(element[0])[:, :, None, None] * running + element[1], running)

    start = jnp.zeros((2, head_count, head_width, state_size), jnp.float32)
    block_states, prefix = lax.scan(
        advance, start, (jnp.swapaxes(totals, 0, 1), jnp.swapaxes(grouped, 0, 1))
    )
    shifted = jnp.concatenate([jnp.zeros((2, 1, head_count), jnp.float32), totals[:, :-1]], axis=1)
    before = jnp.cumsum(shifted, axis=1)
    block_decay = jnp.sum(totals, axis=1)
    entering = carry_by_transpose(block_decay, block_states, "ctx")
    span_enter = jnp.exp(before)[:, :, :, None, None] * entering[:, None] + jnp.swapaxes(
        prefix, 0, 1
    )
    state_bf = span_enter.astype(jnp.bfloat16)
    state_part = jnp.einsum(
        "ktgn,kgqpn->ktgqp", c_spans, state_bf, preferred_element_type=jnp.float32
    )
    state_part = state_part.reshape(span_count, SPAN, head_count, head_width)
    state_part = state_part * jnp.transpose(jnp.exp(cumulative), (1, 2, 0))[:, :, :, None]
    output_rows = (
        diagonal_part + state_part + skip_gain[None, None, :, None] * inputs.astype(jnp.float32)
    )
    return output_rows.reshape(tok_rows, head_count * head_width).astype(jnp.bfloat16)


def solution(mesh):
    placed = (
        P("ctx", "head"),
        P("head", "ctx"),
        P("head", "ctx"),
        P("ctx", "head"),
        P("ctx", "head"),
        P("head"),
    )
    return jax.shard_map(
        on_device, mesh=mesh, in_specs=placed, out_specs=P("ctx", "head"), check_vma=False
    )
```

```python
import jax
import jax.numpy as jnp
import numpy as np
from jax import lax
from jax.sharding import PartitionSpec as P

N = 256
SPAN = 128


def chain_mixing(chain_decay, devices, halves):
    links = halves * devices
    q = np.arange(links)
    between = (q[None, None, :] > q[None, :, None]) & (q[None, None, :] < q[:, None, None])
    gap = jnp.sum(jnp.where(between[None], chain_decay[:, None, None, :], 0.0), axis=-1)
    lower = q[:, None] > q[None, :]
    mixing = jnp.where(lower[None], jnp.exp(gap), 0.0)
    place = np.stack([np.arange(devices), links - 1 - np.arange(devices)], axis=1)
    return mixing[:, place[:, :, None, None], place[None, None, :, :]]


def on_device(features, log_decay, step_size, b_matrix, c_matrix, skip_gain):
    head_count = log_decay.shape[0]
    tok_rows = features.shape[0]
    head_width = features.shape[1] // head_count
    state_size = N
    group_count = b_matrix.shape[1] // state_size
    per_group = head_count // group_count
    halves = tok_rows // SPAN
    assert halves == 2
    devices = lax.axis_size("ctx")
    per_chunk = head_count // devices
    flat = head_width * state_size

    cumulative = jnp.cumsum(log_decay.reshape(head_count, halves, SPAN), axis=2)
    totals = cumulative[:, :, -1]
    got_totals = lax.all_to_all(totals, "ctx", 0, 0, tiled=True)

    step_rows = step_size.reshape(head_count, halves, SPAN)
    grouped_inputs = features.reshape(halves, SPAN, group_count, per_group, head_width)
    b_spans = b_matrix.reshape(halves, SPAN, group_count, state_size)
    c_spans = c_matrix.reshape(halves, SPAN, group_count, state_size)

    coeffs = jnp.exp(totals[:, :, None] - cumulative) * step_rows
    coeffs = jnp.transpose(coeffs.reshape(group_count, per_group, halves, SPAN), (2, 3, 0, 1))
    weighted = (grouped_inputs * coeffs[..., None]).astype(jnp.bfloat16)
    span_states = jnp.einsum(
        "ksgn,ksgqp->gqkpn", b_spans, weighted, preferred_element_type=jnp.float32
    ).reshape(head_count, halves, flat)

    got = lax.all_to_all(span_states, "ctx", 0, 0, tiled=True)
    got = got.reshape(devices, per_chunk, halves, flat)

    chain_decay = got_totals.reshape(devices, per_chunk, halves)
    chain_decay = jnp.concatenate(
        [jnp.transpose(chain_decay[:, :, 0]), jnp.transpose(chain_decay[::-1, :, 1])], axis=1
    )
    mixing = chain_mixing(chain_decay, devices, halves)
    j = np.arange(devices)
    own = np.zeros((devices, halves, devices, halves), bool)
    own[j, 1, j, 0] = True
    own_gain = jnp.sum(jnp.where(own[None], mixing, 0.0), axis=(2, 3, 4))
    solved = jnp.einsum(
        "cjkJL,JcLf->jckf", jnp.where(own[None], 0.0, mixing), got,
        precision=lax.Precision.HIGHEST, preferred_element_type=jnp.float32,
    ).reshape(devices * per_chunk, halves, flat)
    back = lax.all_to_all(solved, "ctx", 0, 0, tiled=True)
    gain = lax.all_to_all(jnp.transpose(own_gain), "ctx", 0, 0, tiled=True).reshape(head_count)
    entering = jnp.stack(
        [back[:, 0], back[:, 1] + gain[:, None] * span_states[:, 0]], axis=1
    )
    state_bf = entering.astype(jnp.bfloat16).reshape(
        group_count, per_group, halves, head_width, state_size
    )

    scores = jnp.einsum("ktgn,ksgn->gkts", c_spans, b_spans, preferred_element_type=jnp.float32)
    causal = jnp.arange(SPAN)[:, None] >= jnp.arange(SPAN)[None, :]
    cum_grouped = cumulative.reshape(group_count, per_group, halves, SPAN)
    step_grouped = step_rows.reshape(group_count, per_group, halves, SPAN)
    decay_gaps = jnp.where(causal, cum_grouped[..., :, None] - cum_grouped[..., None, :], -jnp.inf)
    weights = (scores[:, None] * jnp.exp(decay_gaps) * step_grouped[:, :, :, None, :]).astype(
        jnp.bfloat16
    )
    diagonal_part = jnp.einsum(
        "gqkts,ksgqp->ktgqp", weights, grouped_inputs, preferred_element_type=jnp.float32
    )
    state_part = jnp.einsum(
        "ktgn,gqkpn->ktgqp", c_spans, state_bf, preferred_element_type=jnp.float32
    )
    decay_in = jnp.transpose(jnp.exp(cum_grouped), (2, 3, 0, 1))[..., None]
    skip = skip_gain.reshape(group_count, per_group)[None, None, :, :, None]
    output_rows = (
        diagonal_part + state_part * decay_in + skip * grouped_inputs.astype(jnp.float32)
    )
    return output_rows.reshape(tok_rows, head_count * head_width).astype(jnp.bfloat16)


def solution(mesh):
    placed = (
        P("ctx", "head"),
        P("head", "ctx"),
        P("head", "ctx"),
        P("ctx", "head"),
        P("ctx", "head"),
        P("head"),
    )
    return jax.shard_map(
        on_device, mesh=mesh, in_specs=placed, out_specs=P("ctx", "head"), check_vma=False
    )
```

```python
import jax
import jax.numpy as jnp
import numpy as np
from jax import lax
from jax.sharding import PartitionSpec as P

N = 256
SPAN = 128


def chain_mixing(decay, devices, halves):
    j = np.arange(devices)
    pos = np.stack([j, halves * devices - 1 - j], axis=1).reshape(-1)
    between = (pos[None, :, None] < pos[None, None, :]) & (pos[None, None, :] < pos[:, None, None])
    gap = jnp.sum(jnp.where(between[None], decay[:, None, None, :], 0.0), axis=-1)
    lower = pos[None, :] < pos[:, None]
    mixing = jnp.where(lower[None], jnp.exp(gap), 0.0)
    return mixing.reshape(-1, devices, halves, devices, halves)


def on_device(features, log_decay, step_size, b_matrix, c_matrix, skip_gain):
    head_count = log_decay.shape[0]
    tok_rows = features.shape[0]
    head_width = features.shape[1] // head_count
    state_size = N
    group_count = b_matrix.shape[1] // state_size
    per_group = head_count // group_count
    halves = tok_rows // SPAN
    assert halves == 2
    devices = lax.axis_size("ctx")
    per_chunk = head_count // devices
    flat = head_width * state_size

    rows = halves * head_width
    extra = 8
    cumulative = jnp.cumsum(log_decay.reshape(head_count, halves, SPAN), axis=2)
    totals = cumulative[:, :, -1]

    step_rows = step_size.reshape(head_count, halves, SPAN)
    grouped_inputs = features.reshape(halves, SPAN, group_count, per_group, head_width)
    b_spans = b_matrix.reshape(halves, SPAN, group_count, state_size)
    c_spans = c_matrix.reshape(halves, SPAN, group_count, state_size)

    coeffs = jnp.exp(totals[:, :, None] - cumulative) * step_rows
    coeffs = jnp.transpose(coeffs.reshape(group_count, per_group, halves, SPAN), (2, 3, 0, 1))
    weighted = (grouped_inputs * coeffs[..., None]).astype(jnp.bfloat16)
    span_states = jnp.einsum(
        "ksgn,ksgqp->gqkpn", b_spans, weighted, preferred_element_type=jnp.float32
    ).reshape(head_count, rows, state_size)
    tail = jnp.concatenate(
        [totals, jnp.zeros((head_count, extra - halves), jnp.float32)], axis=1
    )
    payload = jnp.concatenate(
        [span_states, jnp.broadcast_to(tail[:, :, None], (head_count, extra, state_size))], axis=1
    )
    got = lax.all_to_all(payload, "ctx", 0, 0, tiled=True)
    got_states = got[:, :rows].reshape(devices, per_chunk, halves, head_width, state_size)
    got_decay = got[:, rows:rows + halves, 0].reshape(devices, per_chunk, halves)

    mixing = chain_mixing(
        jnp.transpose(got_decay, (1, 0, 2)).reshape(per_chunk, devices * halves), devices, halves
    )
    j = np.arange(devices)
    own = np.zeros((devices, halves, devices, halves), bool)
    own[j, 1, j, 0] = True
    own_gain = jnp.sum(jnp.where(own[None], mixing, 0.0), axis=(3, 4))[:, :, 1]
    solved = jnp.einsum(
        "cjkJL,JcLpn->jckpn", jnp.where(own[None], 0.0, mixing), got_states,
        precision=lax.Precision.HIGHEST, preferred_element_type=jnp.float32,
    ).reshape(devices * per_chunk, rows, state_size)
    gain_rows = jnp.broadcast_to(
        jnp.transpose(own_gain).reshape(devices * per_chunk, 1, 1),
        (devices * per_chunk, extra, state_size),
    )
    back = lax.all_to_all(jnp.concatenate([solved, gain_rows], axis=1), "ctx", 0, 0, tiled=True)
    half_rows = head_width
    gain = back[:, rows:rows + 1, :1]
    entering = jnp.concatenate(
        [
            back[:, :half_rows],
            back[:, half_rows:rows] + gain * span_states[:, :half_rows],
        ],
        axis=1,
    )
    state_bf = entering.astype(jnp.bfloat16).reshape(
        group_count, per_group, halves, head_width, state_size
    )

    scores = jnp.einsum("ktgn,ksgn->gkts", c_spans, b_spans, preferred_element_type=jnp.float32)
    causal = jnp.arange(SPAN)[:, None] >= jnp.arange(SPAN)[None, :]
    cum_grouped = cumulative.reshape(group_count, per_group, halves, SPAN)
    step_grouped = step_rows.reshape(group_count, per_group, halves, SPAN)
    decay_gaps = jnp.where(causal, cum_grouped[..., :, None] - cum_grouped[..., None, :], -jnp.inf)
    weights = (scores[:, None] * jnp.exp(decay_gaps) * step_grouped[:, :, :, None, :]).astype(
        jnp.bfloat16
    )
    diagonal_part = jnp.einsum(
        "gqkts,ksgqp->ktgqp", weights, grouped_inputs, preferred_element_type=jnp.float32
    )
    state_part = jnp.einsum(
        "ktgn,gqkpn->ktgqp", c_spans, state_bf, preferred_element_type=jnp.float32
    )
    decay_in = jnp.transpose(jnp.exp(cum_grouped), (2, 3, 0, 1))[..., None]
    skip = skip_gain.reshape(group_count, per_group)[None, None, :, :, None]
    output_rows = (
        diagonal_part + state_part * decay_in + skip * grouped_inputs.astype(jnp.float32)
    )
    return output_rows.reshape(tok_rows, head_count * head_width).astype(jnp.bfloat16)


def solution(mesh):
    placed = (
        P("ctx", "head"),
        P("head", "ctx"),
        P("head", "ctx"),
        P("ctx", "head"),
        P("ctx", "head"),
        P("head"),
    )
    return jax.shard_map(
        on_device, mesh=mesh, in_specs=placed, out_specs=P("ctx", "head"), check_vma=False
    )
```

```python
import jax
import jax.numpy as jnp
import numpy as np
from jax import lax
from jax.sharding import PartitionSpec as P

N = 256
SPAN = 128
PIECES = 2


def chain_mixing(decay, devices, halves):
    j = np.arange(devices)
    pos = np.stack([j, halves * devices - 1 - j], axis=1).reshape(-1)
    between = (pos[None, :, None] < pos[None, None, :]) & (pos[None, None, :] < pos[:, None, None])
    gap = jnp.sum(jnp.where(between[None], decay[:, None, None, :], 0.0), axis=-1)
    lower = pos[None, :] < pos[:, None]
    mixing = jnp.where(lower[None], jnp.exp(gap), 0.0)
    return mixing.reshape(-1, devices, halves, devices, halves)


def on_device(features, log_decay, step_size, b_matrix, c_matrix, skip_gain):
    head_count = log_decay.shape[0]
    tok_rows = features.shape[0]
    head_width = features.shape[1] // head_count
    state_size = N
    group_count = b_matrix.shape[1] // state_size
    per_group = head_count // group_count
    halves = tok_rows // SPAN
    assert halves == 2
    devices = lax.axis_size("ctx")
    per_chunk = head_count // devices
    flat = head_width * state_size

    rows = halves * head_width
    extra = 8
    cumulative = jnp.cumsum(log_decay.reshape(head_count, halves, SPAN), axis=2)
    totals = cumulative[:, :, -1]

    step_rows = step_size.reshape(head_count, halves, SPAN)
    grouped_inputs = features.reshape(halves, SPAN, group_count, per_group, head_width)
    b_spans = b_matrix.reshape(halves, SPAN, group_count, state_size)
    c_spans = c_matrix.reshape(halves, SPAN, group_count, state_size)

    coeffs = jnp.exp(totals[:, :, None] - cumulative) * step_rows
    coeffs = jnp.transpose(coeffs.reshape(group_count, per_group, halves, SPAN), (2, 3, 0, 1))
    weighted = (grouped_inputs * coeffs[..., None]).astype(jnp.bfloat16)
    span_states = jnp.einsum(
        "ksgn,ksgqp->gqkpn", b_spans, weighted, preferred_element_type=jnp.float32
    ).reshape(head_count, rows, state_size)
    tail = jnp.concatenate(
        [totals, jnp.zeros((head_count, extra - halves), jnp.float32)], axis=1
    )
    tail = jnp.broadcast_to(tail[:, :, None], (head_count, extra, state_size))
    grid = span_states.reshape(head_count, halves, head_width, state_size)
    width = head_width // PIECES
    j = np.arange(devices)
    own = np.zeros((devices, halves, devices, halves), bool)
    own[j, 1, j, 0] = True
    parts = []
    for piece in range(PIECES):
        chunk = grid[:, :, piece * width:(piece + 1) * width].reshape(head_count, halves * width, state_size)
        if piece == 0:
            chunk = jnp.concatenate([chunk, tail], axis=1)
        got = lax.all_to_all(chunk, "ctx", 0, 0, tiled=True)
        got_states = got[:, :halves * width].reshape(devices, per_chunk, halves, width, state_size)
        if piece == 0:
            got_decay = got[:, halves * width:halves * width + halves, 0]
            got_decay = got_decay.reshape(devices, per_chunk, halves)
            mixing = chain_mixing(
                jnp.transpose(got_decay, (1, 0, 2)).reshape(per_chunk, devices * halves),
                devices, halves,
            )
            own_gain = jnp.sum(jnp.where(own[None], mixing, 0.0), axis=(3, 4))[:, :, 1]
            others = jnp.where(own[None], 0.0, mixing)
        solved = jnp.einsum(
            "cjkJL,JcLpn->jckpn", others, got_states,
            precision=lax.Precision.HIGHEST, preferred_element_type=jnp.float32,
        ).reshape(devices * per_chunk, halves * width, state_size)
        gain_rows = jnp.broadcast_to(
            jnp.transpose(own_gain).reshape(devices * per_chunk, 1, 1),
            (devices * per_chunk, extra, state_size),
        )
        back = lax.all_to_all(jnp.concatenate([solved, gain_rows], axis=1), "ctx", 0, 0, tiled=True)
        gain = back[:, halves * width:halves * width + 1, :1]
        back = back[:, :halves * width].reshape(head_count, halves, width, state_size)
        parts.append(
            jnp.stack([back[:, 0], back[:, 1] + gain * grid[:, 0, piece * width:(piece + 1) * width]], axis=1)
        )
    entering = jnp.concatenate(parts, axis=2)
    state_bf = entering.astype(jnp.bfloat16).reshape(
        group_count, per_group, halves, head_width, state_size
    )

    scores = jnp.einsum("ktgn,ksgn->gkts", c_spans, b_spans, preferred_element_type=jnp.float32)
    causal = jnp.arange(SPAN)[:, None] >= jnp.arange(SPAN)[None, :]
    cum_grouped = cumulative.reshape(group_count, per_group, halves, SPAN)
    step_grouped = step_rows.reshape(group_count, per_group, halves, SPAN)
    decay_gaps = jnp.where(causal, cum_grouped[..., :, None] - cum_grouped[..., None, :], -jnp.inf)
    weights = (scores[:, None] * jnp.exp(decay_gaps) * step_grouped[:, :, :, None, :]).astype(
        jnp.bfloat16
    )
    diagonal_part = jnp.einsum(
        "gqkts,ksgqp->ktgqp", weights, grouped_inputs, preferred_element_type=jnp.float32
    )
    state_part = jnp.einsum(
        "ktgn,gqkpn->ktgqp", c_spans, state_bf, preferred_element_type=jnp.float32
    )
    decay_in = jnp.transpose(jnp.exp(cum_grouped), (2, 3, 0, 1))[..., None]
    skip = skip_gain.reshape(group_count, per_group)[None, None, :, :, None]
    output_rows = (
        diagonal_part + state_part * decay_in + skip * grouped_inputs.astype(jnp.float32)
    )
    return output_rows.reshape(tok_rows, head_count * head_width).astype(jnp.bfloat16)


def solution(mesh):
    placed = (
        P("ctx", "head"),
        P("head", "ctx"),
        P("head", "ctx"),
        P("ctx", "head"),
        P("ctx", "head"),
        P("head"),
    )
    return jax.shard_map(
        on_device, mesh=mesh, in_specs=placed, out_specs=P("ctx", "head"), check_vma=False
    )
```

```python
import jax
import jax.numpy as jnp
import numpy as np
from jax import lax
from jax.sharding import PartitionSpec as P

N = 256
SPAN = 128


def chain_mixing(decay, devices, halves):
    j = np.arange(devices)
    pos = np.stack([j, halves * devices - 1 - j], axis=1).reshape(-1)
    between = (pos[None, :, None] < pos[None, None, :]) & (pos[None, None, :] < pos[:, None, None])
    gap = jnp.sum(jnp.where(between[None], decay[:, None, None, :], 0.0), axis=-1)
    lower = pos[None, :] < pos[:, None]
    mixing = jnp.where(lower[None], jnp.exp(gap), 0.0)
    return mixing.reshape(-1, devices, halves, devices, halves)


def on_device(features, log_decay, step_size, b_matrix, c_matrix, skip_gain):
    head_count = log_decay.shape[0]
    tok_rows = features.shape[0]
    head_width = features.shape[1] // head_count
    state_size = N
    group_count = b_matrix.shape[1] // state_size
    per_group = head_count // group_count
    halves = tok_rows // SPAN
    assert halves == 2
    devices = lax.axis_size("ctx")
    per_chunk = head_count // devices
    flat = head_width * state_size

    rows = halves * head_width
    extra = 8
    cumulative = jnp.cumsum(log_decay.reshape(head_count, halves, SPAN), axis=2)
    totals = cumulative[:, :, -1]

    step_rows = step_size.reshape(head_count, halves, SPAN)
    grouped_inputs = features.reshape(halves, SPAN, group_count, per_group, head_width)
    b_spans = b_matrix.reshape(halves, SPAN, group_count, state_size)
    c_spans = c_matrix.reshape(halves, SPAN, group_count, state_size)

    coeffs = jnp.exp(totals[:, :, None] - cumulative) * step_rows
    coeffs = jnp.transpose(coeffs.reshape(group_count, per_group, halves, SPAN), (2, 3, 0, 1))
    weighted = (grouped_inputs * coeffs[..., None]).astype(jnp.bfloat16)
    span_states = jnp.einsum(
        "ksgn,ksgqp->gqkpn", b_spans, weighted, preferred_element_type=jnp.float32
    ).reshape(head_count, rows, state_size)
    tail = jnp.concatenate(
        [totals, jnp.zeros((head_count, extra - halves), jnp.float32)], axis=1
    )
    payload = jnp.concatenate(
        [span_states, jnp.broadcast_to(tail[:, :, None], (head_count, extra, state_size))], axis=1
    )
    got = lax.all_to_all(payload, "ctx", 0, 0, tiled=True)
    got_states = got[:, :rows].reshape(devices, per_chunk, halves, head_width, state_size)
    got_decay = got[:, rows:rows + halves, 0].reshape(devices, per_chunk, halves)

    mixing = chain_mixing(
        jnp.transpose(got_decay, (1, 0, 2)).reshape(per_chunk, devices * halves), devices, halves
    )
    j = np.arange(devices)
    own = np.zeros((devices, halves, devices, halves), bool)
    own[j, 1, j, 0] = True
    own_gain = jnp.sum(jnp.where(own[None], mixing, 0.0), axis=(3, 4))[:, :, 1]
    others = jnp.where(own[None], 0.0, mixing)
    if per_chunk == 1:
        solved = jnp.einsum(
            "uv,vpn->upn", others.reshape(devices * halves, devices * halves),
            got[:, :rows].reshape(devices * halves, head_width, state_size),
            precision=lax.Precision.HIGHEST, preferred_element_type=jnp.float32,
        ).reshape(devices, rows, state_size)
    else:
        solved = jnp.einsum(
            "cjkJL,JcLpn->jckpn", others, got_states,
            precision=lax.Precision.HIGHEST, preferred_element_type=jnp.float32,
        ).reshape(devices * per_chunk, rows, state_size)
    gain_rows = jnp.broadcast_to(
        jnp.transpose(own_gain).reshape(devices * per_chunk, 1, 1),
        (devices * per_chunk, extra, state_size),
    )
    back = lax.all_to_all(jnp.concatenate([solved, gain_rows], axis=1), "ctx", 0, 0, tiled=True)
    gain = back[:, rows:rows + 1, :1]
    front_in = back[:, :head_width]
    back_in = back[:, head_width:rows] + gain * span_states[:, :head_width]
    state_bf = jnp.stack([front_in, back_in]).astype(jnp.bfloat16).reshape(
        halves, group_count, per_group * head_width, state_size
    )

    scores = jnp.einsum("ktgn,ksgn->gkts", c_spans, b_spans, preferred_element_type=jnp.float32)
    causal = jnp.arange(SPAN)[:, None] >= jnp.arange(SPAN)[None, :]
    cum_grouped = cumulative.reshape(group_count, per_group, halves, SPAN)
    step_grouped = step_rows.reshape(group_count, per_group, halves, SPAN)
    decay_gaps = jnp.where(causal, cum_grouped[..., :, None] - cum_grouped[..., None, :], -jnp.inf)
    weights = (scores[:, None] * jnp.exp(decay_gaps) * step_grouped[:, :, :, None, :]).astype(
        jnp.bfloat16
    )
    diagonal_part = jnp.einsum(
        "gqkts,ksgqp->ktgqp", weights, grouped_inputs, preferred_element_type=jnp.float32
    ).reshape(halves, SPAN, head_count * head_width)
    state_part = jnp.einsum(
        "ktgn,kgmn->ktgm", c_spans, state_bf, preferred_element_type=jnp.float32
    ).reshape(halves, SPAN, head_count * head_width)
    decay_in = jnp.broadcast_to(
        jnp.transpose(jnp.exp(cumulative), (1, 2, 0))[..., None],
        (halves, SPAN, head_count, head_width),
    ).reshape(halves, SPAN, head_count * head_width)
    skip = jnp.repeat(skip_gain, head_width)[None, None, :]
    inputs = features.reshape(halves, SPAN, head_count * head_width).astype(jnp.float32)
    output_rows = diagonal_part + state_part * decay_in + skip * inputs
    return output_rows.reshape(tok_rows, head_count * head_width).astype(jnp.bfloat16)


def solution(mesh):
    placed = (
        P("ctx", "head"),
        P("head", "ctx"),
        P("head", "ctx"),
        P("ctx", "head"),
        P("ctx", "head"),
        P("head"),
    )
    return jax.shard_map(
        on_device, mesh=mesh, in_specs=placed, out_specs=P("ctx", "head"), check_vma=False
    )
```

```python
import jax
import jax.numpy as jnp
import numpy as np
from jax import lax
from jax.sharding import PartitionSpec as P

N = 256
SPAN = 128


def chain_mixing(decay, devices, halves):
    j = np.arange(devices)
    pos = np.stack([j, halves * devices - 1 - j], axis=1).reshape(-1)
    between = (pos[None, :, None] < pos[None, None, :]) & (pos[None, None, :] < pos[:, None, None])
    gap = jnp.sum(jnp.where(between[None], decay[:, None, None, :], 0.0), axis=-1)
    lower = pos[None, :] < pos[:, None]
    mixing = jnp.where(lower[None], jnp.exp(gap), 0.0)
    return mixing.reshape(-1, devices, halves, devices, halves)


def on_device(features, log_decay, step_size, b_matrix, c_matrix, skip_gain):
    head_count = log_decay.shape[0]
    tok_rows = features.shape[0]
    head_width = features.shape[1] // head_count
    state_size = N
    group_count = b_matrix.shape[1] // state_size
    per_group = head_count // group_count
    halves = tok_rows // SPAN
    assert halves == 2
    devices = lax.axis_size("ctx")
    per_chunk = head_count // devices
    flat = head_width * state_size

    rows = halves * head_width
    extra = 8
    cumulative = jnp.cumsum(log_decay.reshape(head_count, halves, SPAN), axis=2)
    totals = cumulative[:, :, -1]

    step_rows = step_size.reshape(head_count, halves, SPAN)
    grouped_inputs = features.reshape(halves, SPAN, group_count, per_group, head_width)
    b_spans = b_matrix.reshape(halves, SPAN, group_count, state_size)
    c_spans = c_matrix.reshape(halves, SPAN, group_count, state_size)

    coeffs = jnp.exp(totals[:, :, None] - cumulative) * step_rows
    coeffs = jnp.transpose(coeffs.reshape(group_count, per_group, halves, SPAN), (2, 3, 0, 1))
    weighted = (grouped_inputs * coeffs[..., None]).astype(jnp.bfloat16)
    span_states = jnp.einsum(
        "ksgn,ksgqp->gqkpn", b_spans, weighted, preferred_element_type=jnp.float32
    ).reshape(head_count, rows, state_size)
    tail = jnp.concatenate(
        [totals, jnp.zeros((head_count, extra - halves), jnp.float32)], axis=1
    )
    payload = jnp.concatenate(
        [span_states, jnp.broadcast_to(tail[:, :, None], (head_count, extra, state_size))], axis=1
    )
    got = lax.all_to_all(payload, "ctx", 0, 0, tiled=True)
    got_states = got[:, :rows].reshape(devices, per_chunk, halves, head_width, state_size)
    got_decay = got[:, rows:rows + halves, 0].reshape(devices, per_chunk, halves)

    mixing = chain_mixing(
        jnp.transpose(got_decay, (1, 0, 2)).reshape(per_chunk, devices * halves), devices, halves
    )
    j = np.arange(devices)
    own = np.zeros((devices, halves, devices, halves), bool)
    own[j, 1, j, 0] = True
    own_gain = jnp.sum(jnp.where(own[None], mixing, 0.0), axis=(3, 4))[:, :, 1]
    others = jnp.where(own[None], 0.0, mixing)
    if per_chunk == 1:
        solved = jnp.einsum(
            "uv,vpn->upn", others.reshape(devices * halves, devices * halves),
            got[:, :rows].reshape(devices * halves, head_width, state_size),
            precision=lax.Precision.HIGH, preferred_element_type=jnp.float32,
        ).reshape(devices, rows, state_size)
    else:
        solved = jnp.einsum(
            "cjkJL,JcLpn->jckpn", others, got_states,
            precision=lax.Precision.HIGH, preferred_element_type=jnp.float32,
        ).reshape(devices * per_chunk, rows, state_size)
    gain_rows = jnp.broadcast_to(
        jnp.transpose(own_gain).reshape(devices * per_chunk, 1, 1),
        (devices * per_chunk, extra, state_size),
    )
    back = lax.all_to_all(jnp.concatenate([solved, gain_rows], axis=1), "ctx", 0, 0, tiled=True)
    half_rows = head_width
    gain = back[:, rows:rows + 1, :1]
    entering = jnp.concatenate(
        [
            back[:, :half_rows],
            back[:, half_rows:rows] + gain * span_states[:, :half_rows],
        ],
        axis=1,
    )
    state_bf = entering.astype(jnp.bfloat16).reshape(
        group_count, per_group, halves, head_width, state_size
    )

    scores = jnp.einsum("ktgn,ksgn->gkts", c_spans, b_spans, preferred_element_type=jnp.float32)
    causal = jnp.arange(SPAN)[:, None] >= jnp.arange(SPAN)[None, :]
    cum_grouped = cumulative.reshape(group_count, per_group, halves, SPAN)
    step_grouped = step_rows.reshape(group_count, per_group, halves, SPAN)
    decay_gaps = jnp.where(causal, cum_grouped[..., :, None] - cum_grouped[..., None, :], -jnp.inf)
    weights = (scores[:, None] * jnp.exp(decay_gaps) * step_grouped[:, :, :, None, :]).astype(
        jnp.bfloat16
    )
    diagonal_part = jnp.einsum(
        "gqkts,ksgqp->ktgqp", weights, grouped_inputs, preferred_element_type=jnp.float32
    )
    state_part = jnp.einsum(
        "ktgn,gqkpn->ktgqp", c_spans, state_bf, preferred_element_type=jnp.float32
    )
    decay_in = jnp.transpose(jnp.exp(cum_grouped), (2, 3, 0, 1))[..., None]
    skip = skip_gain.reshape(group_count, per_group)[None, None, :, :, None]
    output_rows = (
        diagonal_part + state_part * decay_in + skip * grouped_inputs.astype(jnp.float32)
    )
    return output_rows.reshape(tok_rows, head_count * head_width).astype(jnp.bfloat16)


def solution(mesh):
    placed = (
        P("ctx", "head"),
        P("head", "ctx"),
        P("head", "ctx"),
        P("ctx", "head"),
        P("ctx", "head"),
        P("head"),
    )
    return jax.shard_map(
        on_device, mesh=mesh, in_specs=placed, out_specs=P("ctx", "head"), check_vma=False
    )
```

```python
import jax
import jax.numpy as jnp
import numpy as np
from jax import lax
from jax.sharding import PartitionSpec as P

N = 256
SPAN = 128


def chain_mixing(decay, devices, halves):
    j = np.arange(devices)
    pos = np.stack([j, halves * devices - 1 - j], axis=1).reshape(-1)
    between = (pos[None, :, None] < pos[None, None, :]) & (pos[None, None, :] < pos[:, None, None])
    gap = jnp.sum(jnp.where(between[None], decay[:, None, None, :], 0.0), axis=-1)
    lower = pos[None, :] < pos[:, None]
    mixing = jnp.where(lower[None], jnp.exp(gap), 0.0)
    return mixing.reshape(-1, devices, halves, devices, halves)


def on_device(features, log_decay, step_size, b_matrix, c_matrix, skip_gain):
    head_count = log_decay.shape[0]
    tok_rows = features.shape[0]
    head_width = features.shape[1] // head_count
    state_size = N
    group_count = b_matrix.shape[1] // state_size
    per_group = head_count // group_count
    halves = tok_rows // SPAN
    assert halves == 2
    devices = lax.axis_size("ctx")
    per_chunk = head_count // devices
    flat = head_width * state_size

    rows = halves * head_width
    extra = 8
    cumulative = jnp.cumsum(log_decay.reshape(head_count, halves, SPAN), axis=2)
    totals = cumulative[:, :, -1]

    step_rows = step_size.reshape(head_count, halves, SPAN)
    grouped_inputs = features.reshape(halves, SPAN, group_count, per_group, head_width)
    b_spans = b_matrix.reshape(halves, SPAN, group_count, state_size)
    c_spans = c_matrix.reshape(halves, SPAN, group_count, state_size)

    coeffs = jnp.exp(totals[:, :, None] - cumulative) * step_rows
    coeffs = jnp.transpose(coeffs.reshape(group_count, per_group, halves, SPAN), (2, 3, 0, 1))
    weighted = (grouped_inputs * coeffs[..., None]).astype(jnp.bfloat16)
    span_states = jnp.einsum(
        "ksgn,ksgqp->gqkpn", b_spans, weighted, preferred_element_type=jnp.float32
    ).reshape(head_count, rows, state_size)
    tail = jnp.zeros((extra, state_size), jnp.float32)
    tail = tail.at[:halves, :head_count].set(jnp.transpose(totals))
    payload = jnp.concatenate(
        [span_states, jnp.broadcast_to(tail[None], (head_count, extra, state_size))], axis=1
    )
    got = lax.all_to_all(payload, "ctx", 0, 0, tiled=True)
    got_states = got[:, :rows].reshape(devices, per_chunk, halves, head_width, state_size)
    all_decay = got[:, rows:rows + halves, :head_count]
    me = lax.axis_index("ctx")
    mine = lax.dynamic_slice_in_dim(all_decay, me * per_chunk, per_chunk, axis=2)

    mixing = chain_mixing(
        jnp.transpose(mine, (2, 0, 1)).reshape(per_chunk, devices * halves), devices, halves
    )
    j = np.arange(devices)
    own = np.zeros((devices, halves, devices, halves), bool)
    own[j, 1, j, 0] = True
    others = jnp.where(own[None], 0.0, mixing)
    if per_chunk == 1:
        solved = jnp.einsum(
            "uv,vpn->upn", others.reshape(devices * halves, devices * halves),
            got[:, :rows].reshape(devices * halves, head_width, state_size),
            precision=lax.Precision.HIGHEST, preferred_element_type=jnp.float32,
        ).reshape(devices, rows, state_size)
    else:
        solved = jnp.einsum(
            "cjkJL,JcLpn->jckpn", others, got_states,
            precision=lax.Precision.HIGHEST, preferred_element_type=jnp.float32,
        ).reshape(devices * per_chunk, rows, state_size)
    back = lax.all_to_all(solved, "ctx", 0, 0, tiled=True)
    later = (np.arange(devices)[:, None] > me)
    gain = jnp.exp(jnp.sum(jnp.where(later, jnp.sum(all_decay, axis=1), 0.0), axis=0))
    half_rows = head_width
    entering = jnp.concatenate(
        [
            back[:, :half_rows],
            back[:, half_rows:rows] + gain[:, None, None] * span_states[:, :half_rows],
        ],
        axis=1,
    )
    state_bf = entering.astype(jnp.bfloat16).reshape(
        group_count, per_group, halves, head_width, state_size
    )

    scores = jnp.einsum("ktgn,ksgn->gkts", c_spans, b_spans, preferred_element_type=jnp.float32)
    causal = jnp.arange(SPAN)[:, None] >= jnp.arange(SPAN)[None, :]
    cum_grouped = cumulative.reshape(group_count, per_group, halves, SPAN)
    step_grouped = step_rows.reshape(group_count, per_group, halves, SPAN)
    decay_gaps = jnp.where(causal, cum_grouped[..., :, None] - cum_grouped[..., None, :], -jnp.inf)
    weights = (scores[:, None] * jnp.exp(decay_gaps) * step_grouped[:, :, :, None, :]).astype(
        jnp.bfloat16
    )
    diagonal_part = jnp.einsum(
        "gqkts,ksgqp->ktgqp", weights, grouped_inputs, preferred_element_type=jnp.float32
    )
    state_part = jnp.einsum(
        "ktgn,gqkpn->ktgqp", c_spans, state_bf, preferred_element_type=jnp.float32
    )
    decay_in = jnp.transpose(jnp.exp(cum_grouped), (2, 3, 0, 1))[..., None]
    skip = skip_gain.reshape(group_count, per_group)[None, None, :, :, None]
    output_rows = (
        diagonal_part + state_part * decay_in + skip * grouped_inputs.astype(jnp.float32)
    )
    return output_rows.reshape(tok_rows, head_count * head_width).astype(jnp.bfloat16)


def solution(mesh):
    placed = (
        P("ctx", "head"),
        P("head", "ctx"),
        P("head", "ctx"),
        P("ctx", "head"),
        P("ctx", "head"),
        P("head"),
    )
    return jax.shard_map(
        on_device, mesh=mesh, in_specs=placed, out_specs=P("ctx", "head"), check_vma=False
    )
```

```python
import jax
import jax.numpy as jnp
import numpy as np
from jax import lax
from jax.sharding import PartitionSpec as P

N = 256
SPAN = 128


def chain_mixing(decay, devices, halves):
    j = np.arange(devices)
    pos = np.stack([j, halves * devices - 1 - j], axis=1).reshape(-1)
    between = (pos[None, :, None] < pos[None, None, :]) & (pos[None, None, :] < pos[:, None, None])
    gap = jnp.sum(jnp.where(between[None], decay[:, None, None, :], 0.0), axis=-1)
    lower = pos[None, :] < pos[:, None]
    mixing = jnp.where(lower[None], jnp.exp(gap), 0.0)
    return mixing.reshape(-1, devices, halves, devices, halves)


def on_device(features, log_decay, step_size, b_matrix, c_matrix, skip_gain):
    head_count = log_decay.shape[0]
    tok_rows = features.shape[0]
    head_width = features.shape[1] // head_count
    state_size = N
    group_count = b_matrix.shape[1] // state_size
    per_group = head_count // group_count
    halves = tok_rows // SPAN
    assert halves == 2
    devices = lax.axis_size("ctx")
    per_chunk = head_count // devices
    flat = head_width * state_size

    rows = halves * head_width
    extra = 8
    cumulative = jnp.cumsum(log_decay.reshape(head_count, halves, SPAN), axis=2)
    totals = cumulative[:, :, -1]

    step_rows = step_size.reshape(head_count, halves, SPAN)
    grouped_inputs = features.reshape(halves, SPAN, group_count, per_group, head_width)
    b_spans = b_matrix.reshape(halves, SPAN, group_count, state_size)
    c_spans = c_matrix.reshape(halves, SPAN, group_count, state_size)

    coeffs = jnp.exp(totals[:, :, None] - cumulative) * step_rows
    coeffs = jnp.transpose(coeffs.reshape(group_count, per_group, halves, SPAN), (2, 3, 0, 1))
    weighted = (grouped_inputs * coeffs[..., None]).astype(jnp.bfloat16)
    span_states = jnp.einsum(
        "ksgn,ksgqp->gqkpn", b_spans, weighted, preferred_element_type=jnp.float32
    ).reshape(head_count, rows, state_size)
    tail = jnp.zeros((extra, state_size), jnp.float32)
    tail = tail.at[:halves, :head_count].set(jnp.transpose(totals))
    payload = jnp.concatenate(
        [span_states, jnp.broadcast_to(tail[None], (head_count, extra, state_size))], axis=1
    )
    got = lax.all_to_all(payload, "ctx", 0, 0, tiled=True)
    got_states = got[:, :rows].reshape(devices, per_chunk, halves, head_width, state_size)
    all_decay = got[:, rows:rows + halves, :head_count]
    me = lax.axis_index("ctx")
    mine = lax.dynamic_slice_in_dim(all_decay, me * per_chunk, per_chunk, axis=2)

    mixing = chain_mixing(
        jnp.transpose(mine, (2, 0, 1)).reshape(per_chunk, devices * halves), devices, halves
    )
    j = np.arange(devices)
    own = np.zeros((devices, halves, devices, halves), bool)
    own[j, 1, j, 0] = True
    others = jnp.where(own[None], 0.0, mixing)
    if per_chunk == 1:
        solved = jnp.einsum(
            "uv,vpn->upn", others.reshape(devices * halves, devices * halves),
            got[:, :rows].reshape(devices * halves, head_width, state_size),
            precision=lax.Precision.HIGHEST, preferred_element_type=jnp.float32,
        ).reshape(devices, rows, state_size)
    else:
        solved = jnp.einsum(
            "cjkJL,JcLpn->jckpn", others, got_states,
            precision=lax.Precision.HIGHEST, preferred_element_type=jnp.float32,
        ).reshape(devices * per_chunk, rows, state_size)
    back = lax.all_to_all(solved, "ctx", 0, 0, tiled=True)
    later = (np.arange(devices)[:, None] > me)
    gain = jnp.exp(jnp.sum(jnp.where(later, jnp.sum(all_decay, axis=1), 0.0), axis=0))
    state_halves = [
        back[:, :head_width].astype(jnp.bfloat16).reshape(head_count * head_width, state_size),
        (back[:, head_width:rows] + gain[:, None, None] * span_states[:, :head_width])
        .astype(jnp.bfloat16).reshape(head_count * head_width, state_size),
    ]

    scores = jnp.einsum("ktgn,ksgn->gkts", c_spans, b_spans, preferred_element_type=jnp.float32)
    causal = jnp.arange(SPAN)[:, None] >= jnp.arange(SPAN)[None, :]
    cum_grouped = cumulative.reshape(group_count, per_group, halves, SPAN)
    step_grouped = step_rows.reshape(group_count, per_group, halves, SPAN)
    decay_gaps = jnp.where(causal, cum_grouped[..., :, None] - cum_grouped[..., None, :], -jnp.inf)
    weights = (scores[:, None] * jnp.exp(decay_gaps) * step_grouped[:, :, :, None, :]).astype(
        jnp.bfloat16
    )
    diagonal_part = jnp.einsum(
        "gqkts,ksgqp->ktgqp", weights, grouped_inputs, preferred_element_type=jnp.float32
    ).reshape(halves, SPAN, head_count * head_width)
    decay_in = jnp.repeat(jnp.transpose(jnp.exp(cumulative), (1, 2, 0)), head_width, axis=2)
    skip = jnp.repeat(skip_gain, head_width)[None, :]
    inputs = features.reshape(halves, SPAN, head_count * head_width).astype(jnp.float32)
    per_group_width = per_group * head_width
    outs = []
    for k in range(halves):
        state_part = jnp.concatenate(
            [
                jnp.dot(
                    c_spans[k, :, g],
                    state_halves[k][g * per_group_width:(g + 1) * per_group_width].T,
                    preferred_element_type=jnp.float32,
                )
                for g in range(group_count)
            ],
            axis=1,
        )
        outs.append(diagonal_part[k] + state_part * decay_in[k] + skip * inputs[k])
    return jnp.concatenate(outs, axis=0).astype(jnp.bfloat16)


def solution(mesh):
    placed = (
        P("ctx", "head"),
        P("head", "ctx"),
        P("head", "ctx"),
        P("ctx", "head"),
        P("ctx", "head"),
        P("head"),
    )
    return jax.shard_map(
        on_device, mesh=mesh, in_specs=placed, out_specs=P("ctx", "head"), check_vma=False
    )
```

```python
import jax
import jax.numpy as jnp
import numpy as np
from jax import lax
from jax.sharding import PartitionSpec as P

N = 256
SPAN = 128


def chain_mixing(decay, devices, halves):
    j = np.arange(devices)
    pos = np.stack([j, halves * devices - 1 - j], axis=1).reshape(-1)
    between = (pos[None, :, None] < pos[None, None, :]) & (pos[None, None, :] < pos[:, None, None])
    gap = jnp.sum(jnp.where(between[None], decay[:, None, None, :], 0.0), axis=-1)
    lower = pos[None, :] < pos[:, None]
    mixing = jnp.where(lower[None], jnp.exp(gap), 0.0)
    return mixing.reshape(-1, devices, halves, devices, halves)


def on_device(features, log_decay, step_size, b_matrix, c_matrix, skip_gain):
    head_count = log_decay.shape[0]
    tok_rows = features.shape[0]
    head_width = features.shape[1] // head_count
    state_size = N
    group_count = b_matrix.shape[1] // state_size
    per_group = head_count // group_count
    halves = tok_rows // SPAN
    assert halves == 2
    devices = lax.axis_size("ctx")
    per_chunk = head_count // devices
    flat = head_width * state_size

    rows = halves * head_width
    extra = 8
    cumulative = jnp.cumsum(log_decay.reshape(head_count, halves, SPAN), axis=2)
    totals = cumulative[:, :, -1]

    step_rows = step_size.reshape(head_count, halves, SPAN)
    grouped_inputs = features.reshape(halves, SPAN, group_count, per_group, head_width)
    b_spans = b_matrix.reshape(halves, SPAN, group_count, state_size)
    c_spans = c_matrix.reshape(halves, SPAN, group_count, state_size)

    coeffs = jnp.exp(totals[:, :, None] - cumulative) * step_rows
    coeffs = jnp.transpose(coeffs.reshape(group_count, per_group, halves, SPAN), (2, 3, 0, 1))
    weighted = (grouped_inputs * coeffs[..., None]).astype(jnp.bfloat16)
    span_states = jnp.einsum(
        "ksgn,ksgqp->gqkpn", b_spans, weighted, preferred_element_type=jnp.float32
    ).reshape(head_count, rows, state_size)
    me = lax.axis_index("ctx")
    spread = jnp.zeros((devices, halves, head_count), jnp.float32)
    spread = lax.dynamic_update_slice_in_dim(spread, jnp.transpose(totals)[None], me, axis=0)
    all_decay = lax.psum(spread, "ctx")
    got = lax.all_to_all(span_states, "ctx", 0, 0, tiled=True)
    got_states = got.reshape(devices, per_chunk, halves, head_width, state_size)
    mine = lax.dynamic_slice_in_dim(all_decay, me * per_chunk, per_chunk, axis=2)

    mixing = chain_mixing(
        jnp.transpose(mine, (2, 0, 1)).reshape(per_chunk, devices * halves), devices, halves
    )
    j = np.arange(devices)
    own = np.zeros((devices, halves, devices, halves), bool)
    own[j, 1, j, 0] = True
    others = jnp.where(own[None], 0.0, mixing)
    if per_chunk == 1:
        solved = jnp.einsum(
            "uv,vpn->upn", others.reshape(devices * halves, devices * halves),
            got.reshape(devices * halves, head_width, state_size),
            precision=lax.Precision.HIGHEST, preferred_element_type=jnp.float32,
        ).reshape(devices, rows, state_size)
    else:
        solved = jnp.einsum(
            "cjkJL,JcLpn->jckpn", others, got_states,
            precision=lax.Precision.HIGHEST, preferred_element_type=jnp.float32,
        ).reshape(devices * per_chunk, rows, state_size)
    back = lax.all_to_all(solved, "ctx", 0, 0, tiled=True)
    later = (np.arange(devices)[:, None] > me)
    gain = jnp.exp(jnp.sum(jnp.where(later, jnp.sum(all_decay, axis=1), 0.0), axis=0))
    state_halves = [
        back[:, :head_width].astype(jnp.bfloat16).reshape(head_count * head_width, state_size),
        (back[:, head_width:rows] + gain[:, None, None] * span_states[:, :head_width])
        .astype(jnp.bfloat16).reshape(head_count * head_width, state_size),
    ]

    scores = jnp.einsum("ktgn,ksgn->gkts", c_spans, b_spans, preferred_element_type=jnp.float32)
    causal = jnp.arange(SPAN)[:, None] >= jnp.arange(SPAN)[None, :]
    cum_grouped = cumulative.reshape(group_count, per_group, halves, SPAN)
    step_grouped = step_rows.reshape(group_count, per_group, halves, SPAN)
    decay_gaps = jnp.where(causal, cum_grouped[..., :, None] - cum_grouped[..., None, :], -jnp.inf)
    weights = (scores[:, None] * jnp.exp(decay_gaps) * step_grouped[:, :, :, None, :]).astype(
        jnp.bfloat16
    )
    diagonal_part = jnp.einsum(
        "gqkts,ksgqp->ktgqp", weights, grouped_inputs, preferred_element_type=jnp.float32
    ).reshape(halves, SPAN, head_count * head_width)
    decay_in = jnp.repeat(jnp.transpose(jnp.exp(cumulative), (1, 2, 0)), head_width, axis=2)
    skip = jnp.repeat(skip_gain, head_width)[None, :]
    inputs = features.reshape(halves, SPAN, head_count * head_width).astype(jnp.float32)
    per_group_width = per_group * head_width
    outs = []
    for k in range(halves):
        state_part = jnp.concatenate(
            [
                jnp.dot(
                    c_spans[k, :, g],
                    state_halves[k][g * per_group_width:(g + 1) * per_group_width].T,
                    preferred_element_type=jnp.float32,
                )
                for g in range(group_count)
            ],
            axis=1,
        )
        outs.append(diagonal_part[k] + state_part * decay_in[k] + skip * inputs[k])
    return jnp.concatenate(outs, axis=0).astype(jnp.bfloat16)


def solution(mesh):
    placed = (
        P("ctx", "head"),
        P("head", "ctx"),
        P("head", "ctx"),
        P("ctx", "head"),
        P("ctx", "head"),
        P("head"),
    )
    return jax.shard_map(
        on_device, mesh=mesh, in_specs=placed, out_specs=P("ctx", "head"), check_vma=False
    )
```

```python
import jax
import jax.numpy as jnp
import numpy as np
from jax import lax
from jax.sharding import PartitionSpec as P

N = 256
SPAN = 128


def chain_mixing(decay, devices, halves):
    j = np.arange(devices)
    pos = np.stack([j, halves * devices - 1 - j], axis=1).reshape(-1)
    between = (pos[None, :, None] < pos[None, None, :]) & (pos[None, None, :] < pos[:, None, None])
    gap = jnp.sum(jnp.where(between[None], decay[:, None, None, :], 0.0), axis=-1)
    lower = pos[None, :] < pos[:, None]
    mixing = jnp.where(lower[None], jnp.exp(gap), 0.0)
    return mixing.reshape(-1, devices, halves, devices, halves)


def on_device(features, log_decay, step_size, b_matrix, c_matrix, skip_gain):
    head_count = log_decay.shape[0]
    tok_rows = features.shape[0]
    head_width = features.shape[1] // head_count
    state_size = N
    group_count = b_matrix.shape[1] // state_size
    per_group = head_count // group_count
    halves = tok_rows // SPAN
    assert halves == 2
    devices = lax.axis_size("ctx")
    per_chunk = head_count // devices
    flat = head_width * state_size

    rows = halves * head_width
    extra = 8
    cumulative = jnp.cumsum(log_decay.reshape(head_count, halves, SPAN), axis=2)
    totals = cumulative[:, :, -1]

    step_rows = step_size.reshape(head_count, halves, SPAN)
    grouped_inputs = features.reshape(halves, SPAN, group_count, per_group, head_width)
    b_spans = b_matrix.reshape(halves, SPAN, group_count, state_size)
    c_spans = c_matrix.reshape(halves, SPAN, group_count, state_size)

    coeffs = jnp.exp(totals[:, :, None] - cumulative) * step_rows
    coeffs = jnp.transpose(coeffs.reshape(group_count, per_group, halves, SPAN), (2, 3, 0, 1))
    weighted = (grouped_inputs * coeffs[..., None]).astype(jnp.bfloat16)
    span_states = jnp.einsum(
        "ksgn,ksgqp->gqkpn", b_spans, weighted, preferred_element_type=jnp.float32
    ).reshape(head_count, rows, state_size)
    tail = jnp.zeros((extra, state_size), jnp.float32)
    tail = tail.at[:halves, :head_count].set(jnp.transpose(totals))
    payload = jnp.concatenate(
        [span_states, jnp.broadcast_to(tail[None], (head_count, extra, state_size))], axis=1
    )
    got = lax.all_to_all(payload, "ctx", 0, 0, tiled=True)
    got_states = got[:, :rows].reshape(devices, per_chunk, halves, head_width, state_size)
    all_decay = got[:, rows:rows + halves, :head_count]
    me = lax.axis_index("ctx")
    mine = lax.dynamic_slice_in_dim(all_decay, me * per_chunk, per_chunk, axis=2)

    mixing = chain_mixing(
        jnp.transpose(mine, (2, 0, 1)).reshape(per_chunk, devices * halves), devices, halves
    )
    j = np.arange(devices)
    own = np.zeros((devices, halves, devices, halves), bool)
    own[j, 1, j, 0] = True
    others = jnp.where(own[None], 0.0, mixing)
    if per_chunk == 1:
        solved = jnp.einsum(
            "uv,vpn->upn", others.reshape(devices * halves, devices * halves),
            got[:, :rows].reshape(devices * halves, head_width, state_size),
            precision=lax.Precision.HIGHEST, preferred_element_type=jnp.float32,
        ).reshape(devices, rows, state_size)
    else:
        solved = jnp.einsum(
            "cjkJL,JcLpn->jckpn", others, got_states,
            precision=lax.Precision.HIGHEST, preferred_element_type=jnp.float32,
        ).reshape(devices * per_chunk, rows, state_size)
    back = lax.all_to_all(solved, "ctx", 0, 0, tiled=True)
    later = (np.arange(devices)[:, None] > me)
    gain = jnp.exp(jnp.sum(jnp.where(later, jnp.sum(all_decay, axis=1), 0.0), axis=0))
    own_front = jnp.einsum(
        "sgn,sgqp->gqpn", b_spans[0], weighted[0], preferred_element_type=jnp.float32
    ).reshape(head_count, head_width, state_size)
    state_halves = [
        back[:, :head_width].astype(jnp.bfloat16).reshape(head_count * head_width, state_size),
        (back[:, head_width:rows] + gain[:, None, None] * own_front)
        .astype(jnp.bfloat16).reshape(head_count * head_width, state_size),
    ]

    scores = jnp.einsum("ktgn,ksgn->gkts", c_spans, b_spans, preferred_element_type=jnp.float32)
    causal = jnp.arange(SPAN)[:, None] >= jnp.arange(SPAN)[None, :]
    cum_grouped = cumulative.reshape(group_count, per_group, halves, SPAN)
    step_grouped = step_rows.reshape(group_count, per_group, halves, SPAN)
    decay_gaps = jnp.where(causal, cum_grouped[..., :, None] - cum_grouped[..., None, :], -jnp.inf)
    weights = (scores[:, None] * jnp.exp(decay_gaps) * step_grouped[:, :, :, None, :]).astype(
        jnp.bfloat16
    )
    diagonal_part = jnp.einsum(
        "gqkts,ksgqp->ktgqp", weights, grouped_inputs, preferred_element_type=jnp.float32
    ).reshape(halves, SPAN, head_count * head_width)
    decay_in = jnp.repeat(jnp.transpose(jnp.exp(cumulative), (1, 2, 0)), head_width, axis=2)
    skip = jnp.repeat(skip_gain, head_width)[None, :]
    inputs = features.reshape(halves, SPAN, head_count * head_width).astype(jnp.float32)
    per_group_width = per_group * head_width
    outs = []
    for k in range(halves):
        state_part = jnp.concatenate(
            [
                jnp.dot(
                    c_spans[k, :, g],
                    state_halves[k][g * per_group_width:(g + 1) * per_group_width].T,
                    preferred_element_type=jnp.float32,
                )
                for g in range(group_count)
            ],
            axis=1,
        )
        outs.append(diagonal_part[k] + state_part * decay_in[k] + skip * inputs[k])
    return jnp.concatenate(outs, axis=0).astype(jnp.bfloat16)


def solution(mesh):
    placed = (
        P("ctx", "head"),
        P("head", "ctx"),
        P("head", "ctx"),
        P("ctx", "head"),
        P("ctx", "head"),
        P("head"),
    )
    return jax.shard_map(
        on_device, mesh=mesh, in_specs=placed, out_specs=P("ctx", "head"), check_vma=False
    )
```

```python
import jax
import jax.numpy as jnp
import numpy as np
from jax import lax
from jax.sharding import PartitionSpec as P

N = 256
SPAN = 128


def chain_mixing(decay, devices, halves):
    j = np.arange(devices)
    pos = np.stack([j, halves * devices - 1 - j], axis=1).reshape(-1)
    between = (pos[None, :, None] < pos[None, None, :]) & (pos[None, None, :] < pos[:, None, None])
    gap = jnp.sum(jnp.where(between[None], decay[:, None, None, :], 0.0), axis=-1)
    lower = pos[None, :] < pos[:, None]
    mixing = jnp.where(lower[None], jnp.exp(gap), 0.0)
    return mixing.reshape(-1, devices, halves, devices, halves)


def on_device(features, log_decay, step_size, b_matrix, c_matrix, skip_gain):
    head_count = log_decay.shape[0]
    tok_rows = features.shape[0]
    head_width = features.shape[1] // head_count
    state_size = N
    group_count = b_matrix.shape[1] // state_size
    per_group = head_count // group_count
    halves = tok_rows // SPAN
    assert halves == 2
    devices = lax.axis_size("ctx")
    per_chunk = head_count // devices
    flat = head_width * state_size

    rows = halves * head_width
    extra = 8
    cumulative = jnp.cumsum(log_decay.reshape(head_count, halves, SPAN), axis=2)
    totals = cumulative[:, :, -1]

    step_rows = step_size.reshape(head_count, halves, SPAN)
    grouped_inputs = features.reshape(halves, SPAN, group_count, per_group, head_width)
    b_spans = b_matrix.reshape(halves, SPAN, group_count, state_size)
    c_spans = c_matrix.reshape(halves, SPAN, group_count, state_size)

    coeffs = jnp.exp(totals[:, :, None] - cumulative) * step_rows
    coeffs = jnp.transpose(coeffs.reshape(group_count, per_group, halves, SPAN), (2, 3, 0, 1))
    weighted = (grouped_inputs * coeffs[..., None]).astype(jnp.bfloat16)
    span_states = jnp.einsum(
        "ksgn,ksgqp->gqkpn", b_spans, weighted, preferred_element_type=jnp.float32
    ).reshape(head_count, rows, state_size)
    decay_out = jnp.broadcast_to(jnp.transpose(totals)[None], (devices, halves, head_count))
    got, all_decay = lax.all_to_all((span_states, decay_out), "ctx", 0, 0, tiled=True)
    got_states = got.reshape(devices, per_chunk, halves, head_width, state_size)
    me = lax.axis_index("ctx")
    mine = lax.dynamic_slice_in_dim(all_decay, me * per_chunk, per_chunk, axis=2)

    mixing = chain_mixing(
        jnp.transpose(mine, (2, 0, 1)).reshape(per_chunk, devices * halves), devices, halves
    )
    j = np.arange(devices)
    own = np.zeros((devices, halves, devices, halves), bool)
    own[j, 1, j, 0] = True
    others = jnp.where(own[None], 0.0, mixing)
    if per_chunk == 1:
        solved = jnp.einsum(
            "uv,vpn->upn", others.reshape(devices * halves, devices * halves),
            got.reshape(devices * halves, head_width, state_size),
            precision=lax.Precision.HIGHEST, preferred_element_type=jnp.float32,
        ).reshape(devices, rows, state_size)
    else:
        solved = jnp.einsum(
            "cjkJL,JcLpn->jckpn", others, got_states,
            precision=lax.Precision.HIGHEST, preferred_element_type=jnp.float32,
        ).reshape(devices * per_chunk, rows, state_size)
    back = lax.all_to_all(solved, "ctx", 0, 0, tiled=True)
    later = (np.arange(devices)[:, None] > me)
    gain = jnp.exp(jnp.sum(jnp.where(later, jnp.sum(all_decay, axis=1), 0.0), axis=0))
    own_front = jnp.einsum(
        "sgn,sgqp->gqpn", b_spans[0], weighted[0], preferred_element_type=jnp.float32
    ).reshape(head_count, head_width, state_size)
    state_halves = [
        back[:, :head_width].astype(jnp.bfloat16).reshape(head_count * head_width, state_size),
        (back[:, head_width:rows] + gain[:, None, None] * own_front)
        .astype(jnp.bfloat16).reshape(head_count * head_width, state_size),
    ]

    scores = jnp.einsum("ktgn,ksgn->gkts", c_spans, b_spans, preferred_element_type=jnp.float32)
    causal = jnp.arange(SPAN)[:, None] >= jnp.arange(SPAN)[None, :]
    cum_grouped = cumulative.reshape(group_count, per_group, halves, SPAN)
    step_grouped = step_rows.reshape(group_count, per_group, halves, SPAN)
    decay_gaps = jnp.where(causal, cum_grouped[..., :, None] - cum_grouped[..., None, :], -jnp.inf)
    weights = (scores[:, None] * jnp.exp(decay_gaps) * step_grouped[:, :, :, None, :]).astype(
        jnp.bfloat16
    )
    diagonal_part = jnp.einsum(
        "gqkts,ksgqp->ktgqp", weights, grouped_inputs, preferred_element_type=jnp.float32
    ).reshape(halves, SPAN, head_count * head_width)
    decay_in = jnp.repeat(jnp.transpose(jnp.exp(cumulative), (1, 2, 0)), head_width, axis=2)
    skip = jnp.repeat(skip_gain, head_width)[None, :]
    inputs = features.reshape(halves, SPAN, head_count * head_width).astype(jnp.float32)
    per_group_width = per_group * head_width
    outs = []
    for k in range(halves):
        state_part = jnp.concatenate(
            [
                jnp.dot(
                    c_spans[k, :, g],
                    state_halves[k][g * per_group_width:(g + 1) * per_group_width].T,
                    preferred_element_type=jnp.float32,
                )
                for g in range(group_count)
            ],
            axis=1,
        )
        outs.append(diagonal_part[k] + state_part * decay_in[k] + skip * inputs[k])
    return jnp.concatenate(outs, axis=0).astype(jnp.bfloat16)


def solution(mesh):
    placed = (
        P("ctx", "head"),
        P("head", "ctx"),
        P("head", "ctx"),
        P("ctx", "head"),
        P("ctx", "head"),
        P("head"),
    )
    return jax.shard_map(
        on_device, mesh=mesh, in_specs=placed, out_specs=P("ctx", "head"), check_vma=False
    )
```

```python
import jax
import jax.numpy as jnp
import numpy as np
from jax import lax
from jax.sharding import PartitionSpec as P

N = 256
SPAN = 128


def chain_mixing(decay, devices, halves):
    j = np.arange(devices)
    pos = np.stack([j, halves * devices - 1 - j], axis=1).reshape(-1)
    between = (pos[None, :, None] < pos[None, None, :]) & (pos[None, None, :] < pos[:, None, None])
    gap = jnp.sum(jnp.where(between[None], decay[:, None, None, :], 0.0), axis=-1)
    lower = pos[None, :] < pos[:, None]
    mixing = jnp.where(lower[None], jnp.exp(gap), 0.0)
    return mixing.reshape(-1, devices, halves, devices, halves)


def on_device(features, log_decay, step_size, b_matrix, c_matrix, skip_gain):
    head_count = log_decay.shape[0]
    tok_rows = features.shape[0]
    head_width = features.shape[1] // head_count
    state_size = N
    group_count = b_matrix.shape[1] // state_size
    per_group = head_count // group_count
    halves = tok_rows // SPAN
    assert halves == 2
    devices = lax.axis_size("ctx")
    per_chunk = head_count // devices
    flat = head_width * state_size

    rows = halves * head_width
    extra = 8
    cumulative = jnp.cumsum(log_decay.reshape(head_count, halves, SPAN), axis=2)
    totals = cumulative[:, :, -1]

    step_rows = step_size.reshape(head_count, halves, SPAN)
    grouped_inputs = features.reshape(halves, SPAN, group_count, per_group, head_width)
    b_spans = b_matrix.reshape(halves, SPAN, group_count, state_size)
    c_spans = c_matrix.reshape(halves, SPAN, group_count, state_size)

    coeffs = jnp.exp(totals[:, :, None] - cumulative) * step_rows
    coeffs = jnp.transpose(coeffs.reshape(group_count, per_group, halves, SPAN), (2, 3, 0, 1))
    weighted = (grouped_inputs * coeffs[..., None]).astype(jnp.bfloat16)
    span_states = jnp.einsum(
        "ksgn,ksgqp->gqkpn", b_spans, weighted, preferred_element_type=jnp.float32
    ).reshape(head_count, rows, state_size)
    decay_out = jnp.broadcast_to(jnp.transpose(totals)[None], (devices, halves, head_count))
    got, all_decay = lax.all_to_all((span_states, decay_out), "ctx", 0, 0, tiled=True)
    got_states = got.reshape(devices, per_chunk, halves, head_width, state_size)
    me = lax.axis_index("ctx")
    mine = lax.dynamic_slice_in_dim(all_decay, me * per_chunk, per_chunk, axis=2)

    mixing = chain_mixing(
        jnp.transpose(mine, (2, 0, 1)).reshape(per_chunk, devices * halves), devices, halves
    )
    j = np.arange(devices)
    own = np.zeros((devices, halves, devices, halves), bool)
    own[j, 1, j, 0] = True
    others = jnp.where(own[None], 0.0, mixing)
    if per_chunk == 1:
        solved = jnp.einsum(
            "uv,vpn->upn", others.reshape(devices * halves, devices * halves),
            got.reshape(devices * halves, head_width, state_size),
            precision=lax.Precision.HIGHEST, preferred_element_type=jnp.float32,
        ).reshape(devices, rows, state_size)
    else:
        solved = jnp.einsum(
            "cjkJL,JcLpn->jckpn", others, got_states,
            precision=lax.Precision.HIGHEST, preferred_element_type=jnp.float32,
        ).reshape(devices * per_chunk, rows, state_size)
    back = lax.all_to_all(solved, "ctx", 0, 0, tiled=True)
    later = (np.arange(devices)[:, None] > me)
    gain = jnp.exp(jnp.sum(jnp.where(later, jnp.sum(all_decay, axis=1), 0.0), axis=0))
    own_front = jnp.einsum(
        "sgn,sgqp->gqpn", b_spans[0], weighted[0], preferred_element_type=jnp.float32
    ).reshape(head_count, head_width, state_size)
    own_gain = jnp.stack([jnp.zeros_like(gain), gain], axis=1)[:, :, None, None]
    entering = back.reshape(head_count, halves, head_width, state_size) + own_gain * own_front[:, None]
    state_bf = jnp.transpose(entering, (1, 0, 2, 3)).astype(jnp.bfloat16).reshape(
        halves, head_count * head_width, state_size
    )

    scores = jnp.einsum("ktgn,ksgn->gkts", c_spans, b_spans, preferred_element_type=jnp.float32)
    causal = jnp.arange(SPAN)[:, None] >= jnp.arange(SPAN)[None, :]
    cum_grouped = cumulative.reshape(group_count, per_group, halves, SPAN)
    step_grouped = step_rows.reshape(group_count, per_group, halves, SPAN)
    decay_gaps = jnp.where(causal, cum_grouped[..., :, None] - cum_grouped[..., None, :], -jnp.inf)
    weights = (scores[:, None] * jnp.exp(decay_gaps) * step_grouped[:, :, :, None, :]).astype(
        jnp.bfloat16
    )
    diagonal_part = jnp.einsum(
        "gqkts,ksgqp->ktgqp", weights, grouped_inputs, preferred_element_type=jnp.float32
    ).reshape(halves, SPAN, head_count * head_width)
    decay_in = jnp.repeat(jnp.transpose(jnp.exp(cumulative), (1, 2, 0)), head_width, axis=2)
    skip = jnp.repeat(skip_gain, head_width)[None, :]
    inputs = features.reshape(halves, SPAN, head_count * head_width).astype(jnp.float32)
    if group_count == 1:
        state_part = jnp.einsum(
            "ktn,kmn->ktm", c_spans[:, :, 0], state_bf, preferred_element_type=jnp.float32
        )
    else:
        state_part = jnp.einsum(
            "ktgn,kgmn->ktgm", c_spans,
            state_bf.reshape(halves, group_count, per_group * head_width, state_size),
            preferred_element_type=jnp.float32,
        ).reshape(halves, SPAN, head_count * head_width)
    output_rows = diagonal_part + state_part * decay_in + skip[None] * inputs
    return output_rows.reshape(tok_rows, head_count * head_width).astype(jnp.bfloat16)


def solution(mesh):
    placed = (
        P("ctx", "head"),
        P("head", "ctx"),
        P("head", "ctx"),
        P("ctx", "head"),
        P("ctx", "head"),
        P("head"),
    )
    return jax.shard_map(
        on_device, mesh=mesh, in_specs=placed, out_specs=P("ctx", "head"), check_vma=False
    )
```
